512 devices in a mesh: gx: 64 (over z, y), gy: 8 (over x, core).
Axes of the slice: x: 4, y: 4, z: 16, core: 2. Of those that a mesh axis runs over, the one named last changes fastest.
Arguments:
- rhs: float32 [64, 8, 128, 128], P('gx', 'gy'), may hold values from -57 to 57
- face_rows: int32 [64, 8, 4, 128], P('gx', 'gy'), may hold values from 0 to 127
- margin_weight: float32 [64, 8, 4, 128], P('gx', 'gy'), may hold values from 0.2 to 1
- local_blocks: bfloat16 [64, 8, 1, 128, 128], P('gx', 'gy'), may hold values from -0.4 to 4.4
- subdomain_inverse: bfloat16 [64, 8, 128, 640], P('gx', 'gy'), may hold values from -0.4 to 1.8
- coarse_basis: bfloat16 [64, 8, 128, 32], P('gx', 'gy'), may hold values from -0.5 to 0.5
- coarse_inverse: bfloat16 [64, 8, 32, 16384], P('gx', 'gy'), may hold values from -0.09765625 to 0.09765625
- coarse_map: int32 [512], replicated, may hold values from 0 to 511, each once
Outputs:
- solution: float32 [64, 8, 128, 128], P('gx', 'gy')
- relative_residual: float32 [128], replicated
The draws below stay inside these ranges and needn't reach their ends.
Inputs may be any that keep to these rules, and one draw needn't show every extreme that they name: `face_rows`: rows of the subdomain, repeats possible. `coarse_map`: every position once.
All inputs are finite; a program needn't handle non-finite values.
Results may differ from the reference program's by a relative error of at most 0.004.
Values may be sent and summed in bfloat16 or wider, within the bound.
No kernel may reach another device: no remote copies, remote signals or barrier semaphores. Data moves between devices by JAX's collectives and lax.ppermute only.
A program may use at most 64 MiB of HBM per device.

```python
import math
import jax
import jax.numpy as jnp
from jax import lax

NLOC = 128
NRHS = 128
H = 128
BK = 128
NCV = 32
NB = 1
NE = 640
NSUB = 512
NCOARSE = 16384
N_GX = 64
N_GY = 8


def draw_rhs(key, part):
    key_base, key_rows = jax.random.split(key, 2)
    full_shape = (N_GX, N_GY, NLOC, NRHS)
    row_scale = jnp.exp(math.log(10.0) * jax.random.uniform(key_rows, (N_GX, N_GY, NLOC, 1), jnp.float32))
    growth = 1.0 + 2.0 * jnp.arange(N_GX, dtype=jnp.float32).reshape(N_GX, 1, 1, 1) / max(N_GX - 1, 1)
    standard = jnp.clip(jax.random.normal(key_base, full_shape, jnp.float32), -5.0, 5.0)
    return (standard * row_scale * growth / 8.0).astype(jnp.float32)


def draw_local_blocks(key, part):
    key_diag, key_noise = jax.random.split(key)
    diagonal = jax.random.uniform(key_diag, (N_GX, N_GY, NB, BK, 1), jnp.float32, 2.0, 4.0)
    noise = jnp.clip(jax.random.normal(key_noise, (N_GX, N_GY, NB, BK, BK), jnp.float32), -5.0, 5.0)
    return (jnp.eye(BK, dtype=jnp.float32) * diagonal + noise * (0.8 / math.sqrt(BK))).astype(jnp.bfloat16)


def draw_subdomain_inverse(key, part):
    key_diag, key_noise = jax.random.split(key)
    diagonal = jax.random.uniform(key_diag, (N_GX, N_GY, NLOC, 1), jnp.float32, 0.6, 1.4)
    noise = jnp.clip(jax.random.normal(key_noise, (N_GX, N_GY, NLOC, NE), jnp.float32), -5.0, 5.0)
    return (jnp.eye(NLOC, NE, dtype=jnp.float32) * diagonal + noise * (0.8 / math.sqrt(NE))).astype(jnp.bfloat16)


def draw_coarse_inverse(key, part):
    noise = jnp.clip(jax.random.normal(key, (N_GX, N_GY, NCV, NCOARSE), jnp.float32), -5.0, 5.0)
    return (noise * (2.5 / math.sqrt(NCOARSE))).astype(jnp.bfloat16)


def plant(array, own_key, smallest, largest):
    longest = array.shape.index(max(array.shape))
    spots = []
    for shift in (0, 1):
        where = [jax.random.randint(jax.random.fold_in(own_key, axis), (), 0, length) for axis, length in enumerate(array.shape)]
        where[longest] = (where[longest] + shift) % array.shape[longest]
        spots.append(tuple(where))
    return array.at[spots[0]].set(smallest).at[spots[1]].set(largest)


def levels(own_key, shape, pieces, smallest, largest):
    factor_of, own = 1.0, jax.random.fold_in(own_key, 6)
    for position, parts in pieces:
        heights = jnp.exp(jax.random.uniform(jax.random.fold_in(own, position), (parts,), jnp.float32, smallest / len(pieces), largest / len(pieces)))
        factor_of = factor_of * jnp.repeat(heights, shape[position] // parts).reshape([-1 if axis == position else 1 for axis in range(len(shape))])
    return factor_of


def centred(stream_key, shape, deviation, most, shards=(), held_as=jnp.bfloat16):
    array = deviation * jax.random.normal(stream_key, shape, jnp.float32)
    if shards:
        array = array * levels(stream_key, shape, shards, -0.22, 0.18)
    return jnp.clip(array, -most, most).astype(held_as)


def setup_inputs(seed: int = 0) -> dict:
    key_list = jax.random.split(jax.random.key(seed), 9)
    rhs = draw_rhs(jax.random.fold_in(key_list[8], 71), 0)
    face_rows = plant(jax.random.randint(key_list[1], (N_GX, N_GY, 4, H), 0, NLOC), jax.random.fold_in(key_list[1], 1), 0, NLOC - 1).astype(jnp.int32)
    margin_weight = jnp.clip(jnp.exp(math.log(1.0) - 1.609438 * jax.random.uniform(key_list[2], (N_GX, N_GY, 4, H), jnp.float32) ** levels(key_list[2], (N_GX, N_GY, 4, H), ((0, 64), (1, 8)), -0.2, 0.2)), 0.2, 1.0)
    local_blocks = draw_local_blocks(jax.random.fold_in(key_list[8], 71), 0)
    subdomain_inverse = draw_subdomain_inverse(jax.random.fold_in(key_list[8], 71), 0)
    coarse_basis = centred(key_list[5], (N_GX, N_GY, NLOC, NCV), NLOC ** -0.5, 0.5, ((0, 64), (1, 8)))
    coarse_inverse = draw_coarse_inverse(jax.random.fold_in(key_list[8], 71), 0)
    coarse_map = jax.random.permutation(key_list[7], NSUB).astype(jnp.int32)
    return dict(rhs=rhs, face_rows=face_rows, margin_weight=margin_weight, local_blocks=local_blocks, subdomain_inverse=subdomain_inverse, coarse_basis=coarse_basis, coarse_inverse=coarse_inverse, coarse_map=coarse_map)


EPSILON = 1e-06

def least_squares(scale_norm, first_dot, first_norm, cross_dot, second_dot, second_norm):
    radius_one = jnp.sqrt(first_dot * first_dot + first_norm * first_norm)
    cosine_one = first_dot / radius_one
    sine_one = first_norm / radius_one
    upper_entry = cosine_one * cross_dot + sine_one * second_dot
    lower_entry = cosine_one * second_dot - sine_one * cross_dot
    radius_two = jnp.sqrt(lower_entry * lower_entry + second_norm * second_norm)
    cosine_two = lower_entry / radius_two
    sine_two = second_norm / radius_two
    weight_two = -cosine_two * sine_one * scale_norm / radius_two
    weight_one = (cosine_one * scale_norm - upper_entry * weight_two) / radius_one
    return (weight_one, weight_two, sine_one * sine_two)

def neighbour_margin(rounded, face_rows):
    face_packs = jax.vmap(jax.vmap(lambda subdomain_field, margin_rows: subdomain_field[margin_rows]))(rounded, face_rows)
    below_first = jnp.concatenate([jnp.zeros_like(face_packs[:1, :, 1]), face_packs[:-1, :, 1]], axis=0)
    above_first = jnp.concatenate([face_packs[1:, :, 0], jnp.zeros_like(face_packs[:1, :, 0])], axis=0)
    below_second = jnp.concatenate([jnp.zeros_like(face_packs[:, :1, 3]), face_packs[:, :-1, 3]], axis=1)
    above_second = jnp.concatenate([face_packs[:, 1:, 2], jnp.zeros_like(face_packs[:, :1, 2])], axis=1)
    return jnp.stack([below_first, above_first, below_second, above_second], axis=2)

def precondition(vector, face_rows, subdomain_inverse, coarse_basis, coarse_inverse, coarse_map):
    rounded = vector.astype(jnp.bfloat16)
    margin = neighbour_margin(rounded, face_rows).reshape(N_GX, N_GY, 4 * H, NRHS)
    extended = jnp.concatenate([rounded, margin], axis=2).reshape(NSUB, NE, NRHS)
    inverse_rows = subdomain_inverse.reshape(NSUB, NLOC, NE)
    local_part = lax.map(lambda operands: jnp.dot(operands[0], operands[1], preferred_element_type=jnp.float32), (inverse_rows, extended))
    basis = coarse_basis.reshape(NSUB, NLOC, NCV)
    flat_field = rounded.reshape(NSUB, NLOC, NRHS)
    residual = lax.map(lambda operands: jnp.dot(operands[0].T, operands[1], preferred_element_type=jnp.float32), (basis, flat_field)).astype(jnp.bfloat16)
    placed = jnp.zeros((NSUB, NCV, NRHS), jnp.bfloat16).at[coarse_map].set(residual).reshape(NCOARSE, NRHS)
    solved = jnp.dot(coarse_inverse.reshape(NCOARSE, NCOARSE), placed, preferred_element_type=jnp.float32).astype(jnp.bfloat16).reshape(NSUB, NCV, NRHS)
    prolonged = lax.map(lambda operands: jnp.dot(operands[0], operands[1], preferred_element_type=jnp.float32), (basis, solved))
    return (local_part + prolonged).reshape(N_GX, N_GY, NLOC, NRHS)

def apply_operator(vector, face_rows, margin_weight, local_blocks):
    rounded = vector.astype(jnp.bfloat16)
    margin = neighbour_margin(rounded, face_rows).astype(jnp.float32)
    shaped = rounded.reshape(N_GX, N_GY, NB, BK, NRHS).astype(jnp.float32)
    own_part = jnp.einsum('xybrc,xybcn->xybrn', local_blocks.astype(jnp.float32), shaped, precision=lax.Precision.HIGHEST).reshape(N_GX, N_GY, NLOC, NRHS)
    weighted = margin_weight[..., None] * margin

    def spread(margin_rows, margin_values):
        return jnp.zeros((NLOC, NRHS), jnp.float32).at[margin_rows.reshape(-1)].add(margin_values.reshape(4 * H, NRHS))
    coupling = jax.vmap(jax.vmap(spread))(face_rows, weighted)
    return own_part - coupling

def column_sum(left_field, right_field):
    return lax.optimization_barrier(jnp.sum(left_field * right_field, axis=(0, 1, 2)))

def reference(rhs, face_rows, margin_weight, local_blocks, subdomain_inverse, coarse_basis, coarse_inverse, coarse_map):
    scale_norm = jnp.sqrt(column_sum(rhs, rhs) + EPSILON)
    krylov_one = rhs / scale_norm
    precond_one = precondition(krylov_one, face_rows, subdomain_inverse, coarse_basis, coarse_inverse, coarse_map)
    applied = apply_operator(precond_one, face_rows, margin_weight, local_blocks)
    first_dot = column_sum(applied, krylov_one)
    remainder = applied - first_dot * krylov_one
    first_norm = jnp.sqrt(column_sum(remainder, remainder) + EPSILON)
    krylov_two = remainder / first_norm
    precond_two = precondition(krylov_two, face_rows, subdomain_inverse, coarse_basis, coarse_inverse, coarse_map)
    applied = apply_operator(precond_two, face_rows, margin_weight, local_blocks)
    cross_dot = column_sum(applied, krylov_one)
    second_dot = column_sum(applied, krylov_two)
    remainder = applied - cross_dot * krylov_one - second_dot * krylov_two
    second_norm = jnp.sqrt(column_sum(remainder, remainder) + EPSILON)
    weight_one, weight_two, relative = least_squares(scale_norm, first_dot, first_norm, cross_dot, second_dot, second_norm)
    solution = weight_one * precond_one + weight_two * precond_two
    return (solution, relative)
```

```python
import jax
import jax.numpy as jnp
from jax import lax
from jax.sharding import PartitionSpec as P

EPSILON = 1e-06


def neighbours(rows, axis):
    count = lax.axis_size(axis)
    up = [(i, i + 1) for i in range(count - 1)]
    down = [(i + 1, i) for i in range(count - 1)]
    return lax.ppermute(rows[1], axis, up), lax.ppermute(rows[0], axis, down)


def exchange(packs):
    below_first, above_first = neighbours(packs[0:2], "gx")
    below_second, above_second = neighbours(packs[2:4], "gy")
    return jnp.stack([below_first, above_first, below_second, above_second], axis=0)


def allsum(value):
    for axis in ("gy", "gx"):
        count = lax.axis_size(axis)
        if count & (count - 1):
            value = lax.psum(value, axis)
            continue
        step = 1
        while step < count:
            value = value + lax.ppermute(value, axis, [(i, i ^ step) for i in range(count)])
            step *= 2
    return value


def least_squares(scale_norm, first_dot, first_norm, cross_dot, second_dot, second_norm):
    radius_one = jnp.sqrt(first_dot * first_dot + first_norm * first_norm)
    cosine_one = first_dot / radius_one
    sine_one = first_norm / radius_one
    upper_entry = cosine_one * cross_dot + sine_one * second_dot
    lower_entry = cosine_one * second_dot - sine_one * cross_dot
    radius_two = jnp.sqrt(lower_entry * lower_entry + second_norm * second_norm)
    cosine_two = lower_entry / radius_two
    sine_two = second_norm / radius_two
    weight_two = -cosine_two * sine_one * scale_norm / radius_two
    weight_one = (cosine_one * scale_norm - upper_entry * weight_two) / radius_one
    return (weight_one, weight_two, sine_one * sine_two)


def on_device(
    rhs,
    face_rows,
    margin_weight,
    local_blocks,
    subdomain_inverse,
    coarse_basis,
    coarse_inverse,
    coarse_map,
):
    right_side = rhs[0, 0]
    margin_rows = face_rows[0, 0]
    margin_weights = margin_weight[0, 0]
    local_block = local_blocks[0, 0]
    inverse_rows = subdomain_inverse[0, 0]
    basis = coarse_basis[0, 0]
    coarse_rows = coarse_inverse[0, 0]
    owned_rows = right_side.shape[0]
    system_count = right_side.shape[1]
    basis_count = basis.shape[1]
    block_rows = local_block.shape[1]
    count_x = lax.axis_size("gx")
    count_y = lax.axis_size("gy")
    gathered_map = coarse_map.reshape(count_x, count_y).T.reshape(-1)
    positions = (
        gathered_map[:, None] * basis_count + jnp.arange(basis_count, dtype=jnp.int32)[None, :]
    ).reshape(-1)
    permuted = jnp.take(coarse_rows, positions, axis=1)

    def margin_of(field):
        return exchange(field[margin_rows])

    def coarse_gather(residual):
        return lax.all_gather(
            lax.all_gather(residual, "gx", axis=0, tiled=True), "gy", axis=0, tiled=True
        )

    def precondition(rounded, margin):
        extended = jnp.concatenate([rounded, margin.reshape(-1, system_count)], axis=0)
        local_part = jnp.dot(inverse_rows, extended, preferred_element_type=jnp.float32)
        residual = lax.dot_general(
            basis, rounded, (((0,), (0,)), ((), ())), preferred_element_type=jnp.float32
        ).astype(jnp.bfloat16)
        solved = jnp.dot(permuted, coarse_gather(residual), preferred_element_type=jnp.float32)
        return local_part + jnp.dot(
            basis, solved.astype(jnp.bfloat16), preferred_element_type=jnp.float32
        )

    def apply_operator(vector):
        rounded = vector.astype(jnp.bfloat16)
        own_part = jnp.einsum(
            "brc,bcn->brn",
            local_block,
            rounded.reshape(-1, block_rows, system_count),
            preferred_element_type=jnp.float32,
        ).reshape(owned_rows, system_count)
        weighted = margin_weights[:, :, None] * margin_of(rounded).astype(jnp.float32)
        coupling = (
            jnp.zeros((owned_rows, system_count), jnp.float32)
            .at[margin_rows.reshape(-1)]
            .add(weighted.reshape(-1, system_count))
        )
        return own_part - coupling

    def column_norm(vector):
        return jnp.sqrt(allsum(jnp.sum(vector * vector, axis=0)) + EPSILON)

    rhs_margin = margin_of(right_side)
    scale_norm = column_norm(right_side)
    krylov_one = right_side / scale_norm
    margin_one = rhs_margin / scale_norm
    precond_one = precondition(krylov_one.astype(jnp.bfloat16), margin_one.astype(jnp.bfloat16))
    applied = apply_operator(precond_one)
    applied_margin = margin_of(applied)
    first_dot = allsum(jnp.sum(applied * krylov_one, axis=0))
    remainder = applied - first_dot * krylov_one
    first_norm = column_norm(remainder)
    krylov_two = remainder / first_norm
    margin_two = (applied_margin - first_dot * margin_one) / first_norm
    precond_two = precondition(krylov_two.astype(jnp.bfloat16), margin_two.astype(jnp.bfloat16))
    applied = apply_operator(precond_two)
    dots = allsum(
        jnp.stack([jnp.sum(applied * krylov_one, axis=0), jnp.sum(applied * krylov_two, axis=0)])
    )
    cross_dot = dots[0]
    second_dot = dots[1]
    remainder = applied - cross_dot * krylov_one - second_dot * krylov_two
    second_norm = column_norm(remainder)
    weight_one, weight_two, relative = least_squares(
        scale_norm, first_dot, first_norm, cross_dot, second_dot, second_norm
    )
    solution = weight_one * precond_one + weight_two * precond_two
    return (solution[None, None], relative)


def solution(mesh):
    return jax.shard_map(
        on_device,
        mesh=mesh,
        in_specs=(
            P("gx", "gy", None, None),
            P("gx", "gy", None, None),
            P("gx", "gy", None, None),
            P("gx", "gy", None, None, None),
            P("gx", "gy", None, None),
            P("gx", "gy", None, None),
            P("gx", "gy", None, None),
            P(),
        ),
        out_specs=(P("gx", "gy", None, None), P()),
        check_vma=False,
    )
```

```python
import jax
import numpy as np
import jax.numpy as jnp
from jax import lax
from jax.sharding import PartitionSpec as P

EPSILON = 1e-06


def neighbours(rows, axis):
    count = lax.axis_size(axis)
    up = [(i, i + 1) for i in range(count - 1)]
    down = [(i + 1, i) for i in range(count - 1)]
    return lax.ppermute(rows[1], axis, up), lax.ppermute(rows[0], axis, down)


def exchange(packs):
    below_first, above_first = neighbours(packs[0:2], "gx")
    below_second, above_second = neighbours(packs[2:4], "gy")
    return jnp.stack([below_first, above_first, below_second, above_second], axis=0)


def allsum(value):
    for axis in ("gy", "gx"):
        count = lax.axis_size(axis)
        if count & (count - 1):
            value = lax.psum(value, axis)
            continue
        step = 1
        while step < count:
            value = value + lax.ppermute(value, axis, [(i, i ^ step) for i in range(count)])
            step *= 2
    return value


GATHER_ROUNDS = (
    ("gx", 32), ("gx", 16), ("gx", 8), ("gx", 4), ("gx", 2), ("gx", 1), ("gy", 4), ("gy", 2), ("gy", 1),
)


def gather_rounds(count_x, count_y):
    sizes = {"gx": count_x, "gy": count_y}
    return tuple((axis, step) for axis, step in GATHER_ROUNDS if step < sizes[axis])


def doubling_gather(block, rounds):
    held = block[None]
    for axis, step in rounds:
        count = lax.axis_size(axis)
        got = lax.ppermute(held, axis, [(i, i ^ step) for i in range(count)])
        upper = (lax.axis_index(axis) // step) % 2 == 1
        held = jnp.where(
            upper, jnp.concatenate([got, held], axis=0), jnp.concatenate([held, got], axis=0)
        )
    return held.reshape(-1, block.shape[-1])


def gathered_order(rounds, count_y):
    order = []
    for position in range(2 ** len(rounds)):
        index = {"gx": 0, "gy": 0}
        for bit, (axis, step) in enumerate(rounds):
            index[axis] += ((position >> bit) & 1) * step
        order.append(index["gx"] * count_y + index["gy"])
    return np.asarray(order, np.int32)


def least_squares(scale_norm, first_dot, first_norm, cross_dot, second_dot, second_norm):
    radius_one = jnp.sqrt(first_dot * first_dot + first_norm * first_norm)
    cosine_one = first_dot / radius_one
    sine_one = first_norm / radius_one
    upper_entry = cosine_one * cross_dot + sine_one * second_dot
    lower_entry = cosine_one * second_dot - sine_one * cross_dot
    radius_two = jnp.sqrt(lower_entry * lower_entry + second_norm * second_norm)
    cosine_two = lower_entry / radius_two
    sine_two = second_norm / radius_two
    weight_two = -cosine_two * sine_one * scale_norm / radius_two
    weight_one = (cosine_one * scale_norm - upper_entry * weight_two) / radius_one
    return (weight_one, weight_two, sine_one * sine_two)


def on_device(
    rhs,
    face_rows,
    margin_weight,
    local_blocks,
    subdomain_inverse,
    coarse_basis,
    coarse_inverse,
    coarse_map,
):
    right_side = rhs[0, 0]
    margin_rows = face_rows[0, 0]
    margin_weights = margin_weight[0, 0]
    local_block = local_blocks[0, 0]
    inverse_rows = subdomain_inverse[0, 0]
    basis = coarse_basis[0, 0]
    coarse_rows = coarse_inverse[0, 0]
    owned_rows = right_side.shape[0]
    system_count = right_side.shape[1]
    basis_count = basis.shape[1]
    block_rows = local_block.shape[1]
    count_x = lax.axis_size("gx")
    count_y = lax.axis_size("gy")
    rounds = gather_rounds(count_x, count_y)
    gathered_map = coarse_map[gathered_order(rounds, count_y)]
    selection = (
        gathered_map[:, None] == jnp.arange(gathered_map.shape[0], dtype=jnp.int32)[None, :]
    ).astype(coarse_rows.dtype)
    permuted = jnp.einsum(
        "bq,rqc->rbc",
        selection,
        coarse_rows.reshape(basis_count, -1, basis_count),
        preferred_element_type=jnp.float32,
    ).astype(coarse_rows.dtype).reshape(basis_count, -1)

    def margin_of(field):
        return exchange(field[margin_rows])

    def coarse_gather(residual):
        return doubling_gather(residual, rounds)

    def precondition(rounded, margin):
        extended = jnp.concatenate([rounded, margin.reshape(-1, system_count)], axis=0)
        local_part = jnp.dot(inverse_rows, extended, preferred_element_type=jnp.float32)
        residual = lax.dot_general(
            basis, rounded, (((0,), (0,)), ((), ())), preferred_element_type=jnp.float32
        ).astype(jnp.bfloat16)
        solved = jnp.dot(permuted, coarse_gather(residual), preferred_element_type=jnp.float32)
        return local_part + jnp.dot(
            basis, solved.astype(jnp.bfloat16), preferred_element_type=jnp.float32
        )

    def apply_operator(vector):
        rounded = vector.astype(jnp.bfloat16)
        own_part = jnp.einsum(
            "brc,bcn->brn",
            local_block,
            rounded.reshape(-1, block_rows, system_count),
            preferred_element_type=jnp.float32,
        ).reshape(owned_rows, system_count)
        weighted = margin_weights[:, :, None] * margin_of(rounded).astype(jnp.float32)
        coupling = (
            jnp.zeros((owned_rows, system_count), jnp.float32)
            .at[margin_rows.reshape(-1)]
            .add(weighted.reshape(-1, system_count))
        )
        return own_part - coupling

    def column_norm(vector):
        return jnp.sqrt(allsum(jnp.sum(vector * vector, axis=0)) + EPSILON)

    rhs_margin = margin_of(right_side)
    scale_norm = column_norm(right_side)
    krylov_one = right_side / scale_norm
    margin_one = rhs_margin / scale_norm
    precond_one = precondition(krylov_one.astype(jnp.bfloat16), margin_one.astype(jnp.bfloat16))
    applied = apply_operator(precond_one)
    applied_margin = margin_of(applied)
    first_dot = allsum(jnp.sum(applied * krylov_one, axis=0))
    remainder = applied - first_dot * krylov_one
    first_norm = column_norm(remainder)
    krylov_two = remainder / first_norm
    margin_two = (applied_margin - first_dot * margin_one) / first_norm
    precond_two = precondition(krylov_two.astype(jnp.bfloat16), margin_two.astype(jnp.bfloat16))
    applied = apply_operator(precond_two)
    dots = allsum(
        jnp.stack([jnp.sum(applied * krylov_one, axis=0), jnp.sum(applied * krylov_two, axis=0)])
    )
    cross_dot = dots[0]
    second_dot = dots[1]
    remainder = applied - cross_dot * krylov_one - second_dot * krylov_two
    second_norm = column_norm(remainder)
    weight_one, weight_two, relative = least_squares(
        scale_norm, first_dot, first_norm, cross_dot, second_dot, second_norm
    )
    solution = weight_one * precond_one + weight_two * precond_two
    return (solution[None, None], relative)


def solution(mesh):
    return jax.shard_map(
        on_device,
        mesh=mesh,
        in_specs=(
            P("gx", "gy", None, None),
            P("gx", "gy", None, None),
            P("gx", "gy", None, None),
            P("gx", "gy", None, None, None),
            P("gx", "gy", None, None),
            P("gx", "gy", None, None),
            P("gx", "gy", None, None),
            P(),
        ),
        out_specs=(P("gx", "gy", None, None), P()),
        check_vma=False,
    )
```

```python
import jax
import numpy as np
import jax.numpy as jnp
from jax import lax
from jax.sharding import PartitionSpec as P

EPSILON = 1e-06
KEPT_SHARE = 1.0 / 64


def neighbours(rows, axis):
    count = lax.axis_size(axis)
    up = [(i, i + 1) for i in range(count - 1)]
    down = [(i + 1, i) for i in range(count - 1)]
    return lax.ppermute(rows[1], axis, up), lax.ppermute(rows[0], axis, down)


def exchange(packs):
    below_first, above_first = neighbours(packs[0:2], "gx")
    below_second, above_second = neighbours(packs[2:4], "gy")
    return jnp.stack([below_first, above_first, below_second, above_second], axis=0)


def allsum(value):
    for axis in ("gy", "gx"):
        count = lax.axis_size(axis)
        if count & (count - 1):
            value = lax.psum(value, axis)
            continue
        step = 1
        while step < count:
            value = value + lax.ppermute(value, axis, [(i, i ^ step) for i in range(count)])
            step *= 2
    return value


GATHER_ROUNDS = (
    ("gx", 32), ("gx", 16), ("gx", 8), ("gx", 4), ("gx", 2), ("gx", 1), ("gy", 4), ("gy", 2), ("gy", 1),
)


def gather_rounds(count_x, count_y):
    sizes = {"gx": count_x, "gy": count_y}
    return tuple((axis, step) for axis, step in GATHER_ROUNDS if step < sizes[axis])


def doubling_gather(block, rounds):
    held = block[None]
    for axis, step in rounds:
        count = lax.axis_size(axis)
        got = lax.ppermute(held, axis, [(i, i ^ step) for i in range(count)])
        upper = (lax.axis_index(axis) // step) % 2 == 1
        held = jnp.where(
            upper, jnp.concatenate([got, held], axis=0), jnp.concatenate([held, got], axis=0)
        )
    return held.reshape(-1, block.shape[-1])


def gathered_order(rounds, count_y):
    order = []
    for position in range(2 ** len(rounds)):
        index = {"gx": 0, "gy": 0}
        for bit, (axis, step) in enumerate(rounds):
            index[axis] += ((position >> bit) & 1) * step
        order.append(index["gx"] * count_y + index["gy"])
    return np.asarray(order, np.int32)


def least_squares(scale_norm, first_dot, first_norm, cross_dot, second_dot, second_norm):
    radius_one = jnp.sqrt(first_dot * first_dot + first_norm * first_norm)
    cosine_one = first_dot / radius_one
    sine_one = first_norm / radius_one
    upper_entry = cosine_one * cross_dot + sine_one * second_dot
    lower_entry = cosine_one * second_dot - sine_one * cross_dot
    radius_two = jnp.sqrt(lower_entry * lower_entry + second_norm * second_norm)
    cosine_two = lower_entry / radius_two
    sine_two = second_norm / radius_two
    weight_two = -cosine_two * sine_one * scale_norm / radius_two
    weight_one = (cosine_one * scale_norm - upper_entry * weight_two) / radius_one
    return (weight_one, weight_two, sine_one * sine_two)


def on_device(
    rhs,
    face_rows,
    margin_weight,
    local_blocks,
    subdomain_inverse,
    coarse_basis,
    coarse_inverse,
    coarse_map,
):
    right_side = rhs[0, 0]
    margin_rows = face_rows[0, 0]
    margin_weights = margin_weight[0, 0]
    local_block = local_blocks[0, 0]
    inverse_rows = subdomain_inverse[0, 0]
    basis = coarse_basis[0, 0]
    coarse_rows = coarse_inverse[0, 0]
    owned_rows = right_side.shape[0]
    system_count = right_side.shape[1]
    basis_count = basis.shape[1]
    block_rows = local_block.shape[1]
    count_x = lax.axis_size("gx")
    count_y = lax.axis_size("gy")
    rounds = gather_rounds(count_x, count_y)
    gathered_map = coarse_map[gathered_order(rounds, count_y)]
    selection = (
        gathered_map[:, None] == jnp.arange(gathered_map.shape[0], dtype=jnp.int32)[None, :]
    ).astype(coarse_rows.dtype)
    permuted = jnp.einsum(
        "bq,rqc->rbc",
        selection,
        coarse_rows.reshape(basis_count, -1, basis_count),
        preferred_element_type=jnp.float32,
    ).astype(coarse_rows.dtype).reshape(basis_count, -1)

    def margin_of(field):
        return exchange(field[margin_rows])

    def coarse_gather(residual):
        return doubling_gather(residual, rounds)

    def precondition(rounded, margin):
        extended = jnp.concatenate([rounded, margin.reshape(-1, system_count)], axis=0)
        local_part = jnp.dot(inverse_rows, extended, preferred_element_type=jnp.float32)
        residual = lax.dot_general(
            basis, rounded, (((0,), (0,)), ((), ())), preferred_element_type=jnp.float32
        ).astype(jnp.bfloat16)
        solved = jnp.dot(permuted, coarse_gather(residual), preferred_element_type=jnp.float32)
        return local_part + jnp.dot(
            basis, solved.astype(jnp.bfloat16), preferred_element_type=jnp.float32
        )

    def apply_operator(vector):
        rounded = vector.astype(jnp.bfloat16)
        own_part = jnp.einsum(
            "brc,bcn->brn",
            local_block,
            rounded.reshape(-1, block_rows, system_count),
            preferred_element_type=jnp.float32,
        ).reshape(owned_rows, system_count)
        weighted = margin_weights[:, :, None] * margin_of(rounded).astype(jnp.float32)
        coupling = (
            jnp.zeros((owned_rows, system_count), jnp.float32)
            .at[margin_rows.reshape(-1)]
            .add(weighted.reshape(-1, system_count))
        )
        return own_part - coupling

    def column_norm(vector):
        return jnp.sqrt(allsum(jnp.sum(vector * vector, axis=0)) + EPSILON)

    def guarded_norm(expanded, whole, remainder):
        kept = jnp.all(jnp.isfinite(expanded) & (expanded >= KEPT_SHARE * whole))
        return lax.cond(
            kept,
            lambda vector: jnp.sqrt(expanded + EPSILON),
            column_norm,
            remainder,
        )

    rhs_margin = margin_of(right_side)
    scale_norm = column_norm(right_side)
    krylov_one = right_side / scale_norm
    margin_one = rhs_margin / scale_norm
    precond_one = precondition(krylov_one.astype(jnp.bfloat16), margin_one.astype(jnp.bfloat16))
    applied = apply_operator(precond_one)
    applied_margin = margin_of(applied)
    sums = allsum(
        jnp.stack(
            [
                jnp.sum(applied * krylov_one, axis=0),
                jnp.sum(applied * applied, axis=0),
                jnp.sum(krylov_one * krylov_one, axis=0),
            ]
        )
    )
    first_dot = sums[0]
    remainder = applied - first_dot * krylov_one
    expanded = sums[1] - 2.0 * first_dot * first_dot + first_dot * first_dot * sums[2]
    first_norm = guarded_norm(expanded, sums[1], remainder)
    krylov_two = remainder / first_norm
    margin_two = (applied_margin - first_dot * margin_one) / first_norm
    precond_two = precondition(krylov_two.astype(jnp.bfloat16), margin_two.astype(jnp.bfloat16))
    applied = apply_operator(precond_two)
    dots = allsum(
        jnp.stack(
            [
                jnp.sum(applied * krylov_one, axis=0),
                jnp.sum(applied * krylov_two, axis=0),
                jnp.sum(applied * applied, axis=0),
                jnp.sum(krylov_one * krylov_one, axis=0),
                jnp.sum(krylov_one * krylov_two, axis=0),
                jnp.sum(krylov_two * krylov_two, axis=0),
            ]
        )
    )
    cross_dot = dots[0]
    second_dot = dots[1]
    remainder = applied - cross_dot * krylov_one - second_dot * krylov_two
    expanded = (
        dots[2]
        - 2.0 * cross_dot * cross_dot
        - 2.0 * second_dot * second_dot
        + cross_dot * cross_dot * dots[3]
        + 2.0 * cross_dot * second_dot * dots[4]
        + second_dot * second_dot * dots[5]
    )
    second_norm = guarded_norm(expanded, dots[2], remainder)
    weight_one, weight_two, relative = least_squares(
        scale_norm, first_dot, first_norm, cross_dot, second_dot, second_norm
    )
    solution = weight_one * precond_one + weight_two * precond_two
    return (solution[None, None], relative)


def solution(mesh):
    return jax.shard_map(
        on_device,
        mesh=mesh,
        in_specs=(
            P("gx", "gy", None, None),
            P("gx", "gy", None, None),
            P("gx", "gy", None, None),
            P("gx", "gy", None, None, None),
            P("gx", "gy", None, None),
            P("gx", "gy", None, None),
            P("gx", "gy", None, None),
            P(),
        ),
        out_specs=(P("gx", "gy", None, None), P()),
        check_vma=False,
    )
```

```python
import jax
import numpy as np
import jax.numpy as jnp
from jax import lax
from jax.sharding import PartitionSpec as P

EPSILON = 1e-06
KEPT_SHARE = 1.0 / 64


def neighbours(rows, axis):
    count = lax.axis_size(axis)
    up = [(i, i + 1) for i in range(count - 1)]
    down = [(i + 1, i) for i in range(count - 1)]
    return lax.ppermute(rows[1], axis, up), lax.ppermute(rows[0], axis, down)


def exchange(packs):
    below_first, above_first = neighbours(packs[0:2], "gx")
    below_second, above_second = neighbours(packs[2:4], "gy")
    return jnp.stack([below_first, above_first, below_second, above_second], axis=0)


def allsum(value):
    for axis in ("gy", "gx"):
        count = lax.axis_size(axis)
        if count & (count - 1):
            value = lax.psum(value, axis)
            continue
        step = 1
        while step < count:
            value = value + lax.ppermute(value, axis, [(i, i ^ step) for i in range(count)])
            step *= 2
    return value


GATHER_ROUNDS = (
    ("gx", 32), ("gx", 16), ("gx", 8), ("gx", 4), ("gx", 2), ("gx", 1), ("gy", 4), ("gy", 2), ("gy", 1),
)


def gather_rounds(count_x, count_y):
    sizes = {"gx": count_x, "gy": count_y}
    return tuple((axis, step) for axis, step in GATHER_ROUNDS if step < sizes[axis])


def doubling_gather(block, rounds):
    held = block[None]
    for axis, step in rounds:
        count = lax.axis_size(axis)
        got = lax.ppermute(held, axis, [(i, i ^ step) for i in range(count)])
        upper = (lax.axis_index(axis) // step) % 2 == 1
        held = jnp.where(
            upper, jnp.concatenate([got, held], axis=0), jnp.concatenate([held, got], axis=0)
        )
    return held.reshape(-1, block.shape[-1])


def gathered_order(rounds, count_y):
    order = []
    for position in range(2 ** len(rounds)):
        index = {"gx": 0, "gy": 0}
        for bit, (axis, step) in enumerate(rounds):
            index[axis] += ((position >> bit) & 1) * step
        order.append(index["gx"] * count_y + index["gy"])
    return np.asarray(order, np.int32)


def least_squares(scale_norm, first_dot, first_norm, cross_dot, second_dot, second_norm):
    radius_one = jnp.sqrt(first_dot * first_dot + first_norm * first_norm)
    cosine_one = first_dot / radius_one
    sine_one = first_norm / radius_one
    upper_entry = cosine_one * cross_dot + sine_one * second_dot
    lower_entry = cosine_one * second_dot - sine_one * cross_dot
    radius_two = jnp.sqrt(lower_entry * lower_entry + second_norm * second_norm)
    cosine_two = lower_entry / radius_two
    sine_two = second_norm / radius_two
    weight_two = -cosine_two * sine_one * scale_norm / radius_two
    weight_one = (cosine_one * scale_norm - upper_entry * weight_two) / radius_one
    return (weight_one, weight_two, sine_one * sine_two)


def on_device(
    rhs,
    face_rows,
    margin_weight,
    local_blocks,
    subdomain_inverse,
    coarse_basis,
    coarse_inverse,
    coarse_map,
):
    right_side = rhs[0, 0]
    margin_rows = face_rows[0, 0]
    margin_weights = margin_weight[0, 0]
    local_block = local_blocks[0, 0]
    inverse_rows = subdomain_inverse[0, 0]
    basis = coarse_basis[0, 0]
    coarse_rows = coarse_inverse[0, 0]
    owned_rows = right_side.shape[0]
    system_count = right_side.shape[1]
    basis_count = basis.shape[1]
    block_rows = local_block.shape[1]
    count_x = lax.axis_size("gx")
    count_y = lax.axis_size("gy")
    rounds = gather_rounds(count_x, count_y)
    gathered_map = coarse_map[gathered_order(rounds, count_y)]
    selection = (
        gathered_map[:, None] == jnp.arange(gathered_map.shape[0], dtype=jnp.int32)[None, :]
    ).astype(jnp.bfloat16)

    def margin_of(field):
        return exchange(field[margin_rows])

    def coarse_gather(residual):
        return doubling_gather(residual, rounds)

    def precondition(rounded, margin):
        extended = jnp.concatenate([rounded, margin.reshape(-1, system_count)], axis=0)
        local_part = jnp.dot(inverse_rows, extended, preferred_element_type=jnp.float32)
        residual = lax.dot_general(
            basis, rounded, (((0,), (0,)), ((), ())), preferred_element_type=jnp.float32
        ).astype(jnp.bfloat16)
        gathered = coarse_gather(residual).reshape(selection.shape[0], -1)
        placed = lax.dot_general(
            selection, gathered, (((0,), (0,)), ((), ())), preferred_element_type=jnp.float32
        ).astype(jnp.bfloat16)
        solved = jnp.dot(
            coarse_rows, placed.reshape(-1, system_count), preferred_element_type=jnp.float32
        )
        return local_part + jnp.dot(
            basis, solved.astype(jnp.bfloat16), preferred_element_type=jnp.float32
        )

    def apply_operator(vector):
        rounded = vector.astype(jnp.bfloat16)
        own_part = jnp.einsum(
            "brc,bcn->brn",
            local_block,
            rounded.reshape(-1, block_rows, system_count),
            preferred_element_type=jnp.float32,
        ).reshape(owned_rows, system_count)
        weighted = margin_weights[:, :, None] * margin_of(rounded).astype(jnp.float32)
        coupling = (
            jnp.zeros((owned_rows, system_count), jnp.float32)
            .at[margin_rows.reshape(-1)]
            .add(weighted.reshape(-1, system_count))
        )
        return own_part - coupling

    def column_norm(vector):
        return jnp.sqrt(allsum(jnp.sum(vector * vector, axis=0)) + EPSILON)

    def guarded_norm(expanded, whole, remainder):
        kept = jnp.all(jnp.isfinite(expanded) & (expanded >= KEPT_SHARE * whole))
        return lax.cond(
            kept,
            lambda vector: jnp.sqrt(expanded + EPSILON),
            column_norm,
            remainder,
        )

    rhs_margin = margin_of(right_side)
    scale_norm = column_norm(right_side)
    krylov_one = right_side / scale_norm
    margin_one = rhs_margin / scale_norm
    precond_one = precondition(krylov_one.astype(jnp.bfloat16), margin_one.astype(jnp.bfloat16))
    applied = apply_operator(precond_one)
    applied_margin = margin_of(applied)
    sums = allsum(
        jnp.stack(
            [
                jnp.sum(applied * krylov_one, axis=0),
                jnp.sum(applied * applied, axis=0),
                jnp.sum(krylov_one * krylov_one, axis=0),
            ]
        )
    )
    first_dot = sums[0]
    remainder = applied - first_dot * krylov_one
    expanded = sums[1] - 2.0 * first_dot * first_dot + first_dot * first_dot * sums[2]
    first_norm = guarded_norm(expanded, sums[1], remainder)
    krylov_two = remainder / first_norm
    margin_two = (applied_margin - first_dot * margin_one) / first_norm
    precond_two = precondition(krylov_two.astype(jnp.bfloat16), margin_two.astype(jnp.bfloat16))
    applied = apply_operator(precond_two)
    dots = allsum(
        jnp.stack(
            [
                jnp.sum(applied * krylov_one, axis=0),
                jnp.sum(applied * krylov_two, axis=0),
                jnp.sum(applied * applied, axis=0),
                jnp.sum(krylov_one * krylov_one, axis=0),
                jnp.sum(krylov_one * krylov_two, axis=0),
                jnp.sum(krylov_two * krylov_two, axis=0),
            ]
        )
    )
    cross_dot = dots[0]
    second_dot = dots[1]
    remainder = applied - cross_dot * krylov_one - second_dot * krylov_two
    expanded = (
        dots[2]
        - 2.0 * cross_dot * cross_dot
        - 2.0 * second_dot * second_dot
        + cross_dot * cross_dot * dots[3]
        + 2.0 * cross_dot * second_dot * dots[4]
        + second_dot * second_dot * dots[5]
    )
    second_norm = guarded_norm(expanded, dots[2], remainder)
    weight_one, weight_two, relative = least_squares(
        scale_norm, first_dot, first_norm, cross_dot, second_dot, second_norm
    )
    solution = weight_one * precond_one + weight_two * precond_two
    return (solution[None, None], relative)


def solution(mesh):
    return jax.shard_map(
        on_device,
        mesh=mesh,
        in_specs=(
            P("gx", "gy", None, None),
            P("gx", "gy", None, None),
            P("gx", "gy", None, None),
            P("gx", "gy", None, None, None),
            P("gx", "gy", None, None),
            P("gx", "gy", None, None),
            P("gx", "gy", None, None),
            P(),
        ),
        out_specs=(P("gx", "gy", None, None), P()),
        check_vma=False,
    )
```

```python
import jax
import numpy as np
import jax.numpy as jnp
from jax import lax
from jax.sharding import PartitionSpec as P

EPSILON = 1e-06
KEPT_SHARE = 1.0 / 64


def neighbours(rows, axis):
    count = lax.axis_size(axis)
    up = [(i, i + 1) for i in range(count - 1)]
    down = [(i + 1, i) for i in range(count - 1)]
    return lax.ppermute(rows[1], axis, up), lax.ppermute(rows[0], axis, down)


def exchange(packs):
    below_first, above_first = neighbours(packs[0:2], "gx")
    below_second, above_second = neighbours(packs[2:4], "gy")
    return jnp.stack([below_first, above_first, below_second, above_second], axis=0)


def allsum(value):
    for axis in ("gy", "gx"):
        count = lax.axis_size(axis)
        if count & (count - 1):
            value = lax.psum(value, axis)
            continue
        step = 1
        while step < count:
            value = value + lax.ppermute(value, axis, [(i, i ^ step) for i in range(count)])
            step *= 2
    return value


GATHER_ROUNDS = (
    ("gx", 32), ("gx", 16), ("gx", 8), ("gx", 4), ("gx", 2), ("gx", 1), ("gy", 4), ("gy", 2), ("gy", 1),
)


def gather_rounds(count_x, count_y):
    sizes = {"gx": count_x, "gy": count_y}
    return tuple((axis, step) for axis, step in GATHER_ROUNDS if step < sizes[axis])


def doubling_gather(block, rounds):
    held = block[None]
    for axis, step in rounds:
        count = lax.axis_size(axis)
        got = lax.ppermute(held, axis, [(i, i ^ step) for i in range(count)])
        upper = (lax.axis_index(axis) // step) % 2 == 1
        held = jnp.where(
            upper, jnp.concatenate([got, held], axis=0), jnp.concatenate([held, got], axis=0)
        )
    return held.reshape(-1, block.shape[-1])


def gathered_order(rounds, count_y):
    order = []
    for position in range(2 ** len(rounds)):
        index = {"gx": 0, "gy": 0}
        for bit, (axis, step) in enumerate(rounds):
            index[axis] += ((position >> bit) & 1) * step
        order.append(index["gx"] * count_y + index["gy"])
    return np.asarray(order, np.int32)


def least_squares(scale_norm, first_dot, first_norm, cross_dot, second_dot, second_norm):
    radius_one = jnp.sqrt(first_dot * first_dot + first_norm * first_norm)
    cosine_one = first_dot / radius_one
    sine_one = first_norm / radius_one
    upper_entry = cosine_one * cross_dot + sine_one * second_dot
    lower_entry = cosine_one * second_dot - sine_one * cross_dot
    radius_two = jnp.sqrt(lower_entry * lower_entry + second_norm * second_norm)
    cosine_two = lower_entry / radius_two
    sine_two = second_norm / radius_two
    weight_two = -cosine_two * sine_one * scale_norm / radius_two
    weight_one = (cosine_one * scale_norm - upper_entry * weight_two) / radius_one
    return (weight_one, weight_two, sine_one * sine_two)


def on_device(
    rhs,
    face_rows,
    margin_weight,
    local_blocks,
    subdomain_inverse,
    coarse_basis,
    coarse_inverse,
    coarse_map,
):
    right_side = rhs[0, 0]
    margin_rows = face_rows[0, 0]
    margin_weights = margin_weight[0, 0]
    local_block = local_blocks[0, 0]
    inverse_rows = subdomain_inverse[0, 0]
    basis = coarse_basis[0, 0]
    coarse_rows = coarse_inverse[0, 0]
    owned_rows = right_side.shape[0]
    system_count = right_side.shape[1]
    basis_count = basis.shape[1]
    block_rows = local_block.shape[1]
    count_x = lax.axis_size("gx")
    count_y = lax.axis_size("gy")
    rounds = gather_rounds(count_x, count_y)
    gathered_map = coarse_map[gathered_order(rounds, count_y)]
    selection = (
        gathered_map[:, None] == jnp.arange(gathered_map.shape[0], dtype=jnp.int32)[None, :]
    ).astype(jnp.bfloat16)

    def margin_of(field):
        return exchange(field[margin_rows])

    def coarse_gather(residual):
        return doubling_gather(residual, rounds)

    def precondition(rounded, margin):
        extended = jnp.concatenate([rounded, margin.reshape(-1, system_count)], axis=0)
        local_part = jnp.dot(inverse_rows, extended, preferred_element_type=jnp.float32)
        residual = lax.dot_general(
            basis, rounded, (((0,), (0,)), ((), ())), preferred_element_type=jnp.float32
        ).astype(jnp.bfloat16)
        gathered = coarse_gather(residual).reshape(selection.shape[0], basis_count, system_count)
        placed = jnp.einsum(
            "bq,bck->qck", selection, gathered, preferred_element_type=jnp.float32
        ).astype(jnp.bfloat16)
        solved = jnp.dot(
            coarse_rows, placed.reshape(-1, system_count), preferred_element_type=jnp.float32
        )
        return local_part + jnp.dot(
            basis, solved.astype(jnp.bfloat16), preferred_element_type=jnp.float32
        )

    def apply_operator(vector):
        rounded = vector.astype(jnp.bfloat16)
        own_part = jnp.einsum(
            "brc,bcn->brn",
            local_block,
            rounded.reshape(-1, block_rows, system_count),
            preferred_element_type=jnp.float32,
        ).reshape(owned_rows, system_count)
        weighted = margin_weights[:, :, None] * margin_of(rounded).astype(jnp.float32)
        coupling = (
            jnp.zeros((owned_rows, system_count), jnp.float32)
            .at[margin_rows.reshape(-1)]
            .add(weighted.reshape(-1, system_count))
        )
        return own_part - coupling

    def column_norm(vector):
        return jnp.sqrt(allsum(jnp.sum(vector * vector, axis=0)) + EPSILON)

    def guarded_norm(expanded, whole, remainder):
        kept = jnp.all(jnp.isfinite(expanded) & (expanded >= KEPT_SHARE * whole))
        return lax.cond(
            kept,
            lambda vector: jnp.sqrt(expanded + EPSILON),
            column_norm,
            remainder,
        )

    rhs_margin = margin_of(right_side)
    scale_norm = column_norm(right_side)
    krylov_one = right_side / scale_norm
    margin_one = rhs_margin / scale_norm
    precond_one = precondition(krylov_one.astype(jnp.bfloat16), margin_one.astype(jnp.bfloat16))
    applied = apply_operator(precond_one)
    applied_margin = margin_of(applied)
    sums = allsum(
        jnp.stack(
            [
                jnp.sum(applied * krylov_one, axis=0),
                jnp.sum(applied * applied, axis=0),
                jnp.sum(krylov_one * krylov_one, axis=0),
            ]
        )
    )
    first_dot = sums[0]
    remainder = applied - first_dot * krylov_one
    expanded = sums[1] - 2.0 * first_dot * first_dot + first_dot * first_dot * sums[2]
    first_norm = guarded_norm(expanded, sums[1], remainder)
    krylov_two = remainder / first_norm
    margin_two = (applied_margin - first_dot * margin_one) / first_norm
    precond_two = precondition(krylov_two.astype(jnp.bfloat16), margin_two.astype(jnp.bfloat16))
    applied = apply_operator(precond_two)
    dots = allsum(
        jnp.stack(
            [
                jnp.sum(applied * krylov_one, axis=0),
                jnp.sum(applied * krylov_two, axis=0),
                jnp.sum(applied * applied, axis=0),
                jnp.sum(krylov_one * krylov_one, axis=0),
                jnp.sum(krylov_one * krylov_two, axis=0),
                jnp.sum(krylov_two * krylov_two, axis=0),
            ]
        )
    )
    cross_dot = dots[0]
    second_dot = dots[1]
    remainder = applied - cross_dot * krylov_one - second_dot * krylov_two
    expanded = (
        dots[2]
        - 2.0 * cross_dot * cross_dot
        - 2.0 * second_dot * second_dot
        + cross_dot * cross_dot * dots[3]
        + 2.0 * cross_dot * second_dot * dots[4]
        + second_dot * second_dot * dots[5]
    )
    second_norm = guarded_norm(expanded, dots[2], remainder)
    weight_one, weight_two, relative = least_squares(
        scale_norm, first_dot, first_norm, cross_dot, second_dot, second_norm
    )
    solution = weight_one * precond_one + weight_two * precond_two
    return (solution[None, None], relative)


def solution(mesh):
    return jax.shard_map(
        on_device,
        mesh=mesh,
        in_specs=(
            P("gx", "gy", None, None),
            P("gx", "gy", None, None),
            P("gx", "gy", None, None),
            P("gx", "gy", None, None, None),
            P("gx", "gy", None, None),
            P("gx", "gy", None, None),
            P("gx", "gy", None, None),
            P(),
        ),
        out_specs=(P("gx", "gy", None, None), P()),
        check_vma=False,
    )
```

```python
import jax
import numpy as np
import jax.numpy as jnp
from jax import lax
from jax.sharding import PartitionSpec as P

EPSILON = 1e-06
KEPT_SHARE = 1.0 / 64


def neighbours(rows, axis):
    count = lax.axis_size(axis)
    up = [(i, i + 1) for i in range(count - 1)]
    down = [(i + 1, i) for i in range(count - 1)]
    return lax.ppermute(rows[1], axis, up), lax.ppermute(rows[0], axis, down)


def exchange(packs):
    below_first, above_first = neighbours(packs[0:2], "gx")
    below_second, above_second = neighbours(packs[2:4], "gy")
    return jnp.stack([below_first, above_first, below_second, above_second], axis=0)


def allsum(value):
    value = lax.psum(value, "gy")
    for axis in ("gx",):
        count = lax.axis_size(axis)
        if count & (count - 1):
            value = lax.psum(value, axis)
            continue
        step = 1
        while step < count:
            value = value + lax.ppermute(value, axis, [(i, i ^ step) for i in range(count)])
            step *= 2
    return value


GATHER_ROUNDS = (
    ("gx", 32), ("gx", 16), ("gx", 8), ("gx", 4), ("gx", 2), ("gx", 1), ("gy", 4), ("gy", 2), ("gy", 1),
)


def gather_rounds(count_x, count_y):
    sizes = {"gx": count_x, "gy": count_y}
    return tuple((axis, step) for axis, step in GATHER_ROUNDS if step < sizes[axis])


def doubling_gather(block, rounds):
    held = block[None]
    for axis, step in rounds:
        count = lax.axis_size(axis)
        got = lax.ppermute(held, axis, [(i, i ^ step) for i in range(count)])
        upper = (lax.axis_index(axis) // step) % 2 == 1
        held = jnp.where(
            upper, jnp.concatenate([got, held], axis=0), jnp.concatenate([held, got], axis=0)
        )
    return held.reshape(-1, block.shape[-1])


def gathered_order(rounds, count_y):
    order = []
    for position in range(2 ** len(rounds)):
        index = {"gx": 0, "gy": 0}
        for bit, (axis, step) in enumerate(rounds):
            index[axis] += ((position >> bit) & 1) * step
        order.append(index["gx"] * count_y + index["gy"])
    return np.asarray(order, np.int32)


def least_squares(scale_norm, first_dot, first_norm, cross_dot, second_dot, second_norm):
    radius_one = jnp.sqrt(first_dot * first_dot + first_norm * first_norm)
    cosine_one = first_dot / radius_one
    sine_one = first_norm / radius_one
    upper_entry = cosine_one * cross_dot + sine_one * second_dot
    lower_entry = cosine_one * second_dot - sine_one * cross_dot
    radius_two = jnp.sqrt(lower_entry * lower_entry + second_norm * second_norm)
    cosine_two = lower_entry / radius_two
    sine_two = second_norm / radius_two
    weight_two = -cosine_two * sine_one * scale_norm / radius_two
    weight_one = (cosine_one * scale_norm - upper_entry * weight_two) / radius_one
    return (weight_one, weight_two, sine_one * sine_two)


def on_device(
    rhs,
    face_rows,
    margin_weight,
    local_blocks,
    subdomain_inverse,
    coarse_basis,
    coarse_inverse,
    coarse_map,
):
    right_side = rhs[0, 0]
    margin_rows = face_rows[0, 0]
    margin_weights = margin_weight[0, 0]
    local_block = local_blocks[0, 0]
    inverse_rows = subdomain_inverse[0, 0]
    basis = coarse_basis[0, 0]
    coarse_rows = coarse_inverse[0, 0]
    owned_rows = right_side.shape[0]
    system_count = right_side.shape[1]
    basis_count = basis.shape[1]
    block_rows = local_block.shape[1]
    count_x = lax.axis_size("gx")
    count_y = lax.axis_size("gy")
    rounds = gather_rounds(count_x, count_y)
    gathered_map = coarse_map[gathered_order(rounds, count_y)]
    selection = (
        gathered_map[:, None] == jnp.arange(gathered_map.shape[0], dtype=jnp.int32)[None, :]
    ).astype(jnp.bfloat16)

    def margin_of(field):
        return exchange(field[margin_rows])

    def coarse_gather(residual):
        return doubling_gather(residual, rounds)

    def precondition(rounded, margin):
        extended = jnp.concatenate([rounded, margin.reshape(-1, system_count)], axis=0)
        local_part = jnp.dot(inverse_rows, extended, preferred_element_type=jnp.float32)
        residual = lax.dot_general(
            basis, rounded, (((0,), (0,)), ((), ())), preferred_element_type=jnp.float32
        ).astype(jnp.bfloat16)
        gathered = coarse_gather(residual).reshape(selection.shape[0], -1)
        placed = lax.dot_general(
            selection, gathered, (((0,), (0,)), ((), ())), preferred_element_type=jnp.float32
        ).astype(jnp.bfloat16)
        solved = jnp.dot(
            coarse_rows, placed.reshape(-1, system_count), preferred_element_type=jnp.float32
        )
        return local_part + jnp.dot(
            basis, solved.astype(jnp.bfloat16), preferred_element_type=jnp.float32
        )

    def apply_operator(vector):
        rounded = vector.astype(jnp.bfloat16)
        own_part = jnp.einsum(
            "brc,bcn->brn",
            local_block,
            rounded.reshape(-1, block_rows, system_count),
            preferred_element_type=jnp.float32,
        ).reshape(owned_rows, system_count)
        weighted = margin_weights[:, :, None] * margin_of(rounded).astype(jnp.float32)
        coupling = (
            jnp.zeros((owned_rows, system_count), jnp.float32)
            .at[margin_rows.reshape(-1)]
            .add(weighted.reshape(-1, system_count))
        )
        return own_part - coupling

    def column_norm(vector):
        return jnp.sqrt(allsum(jnp.sum(vector * vector, axis=0)) + EPSILON)

    def guarded_norm(expanded, whole, remainder):
        kept = jnp.all(jnp.isfinite(expanded) & (expanded >= KEPT_SHARE * whole))
        return lax.cond(
            kept,
            lambda vector: jnp.sqrt(expanded + EPSILON),
            column_norm,
            remainder,
        )

    rhs_margin = margin_of(right_side)
    scale_norm = column_norm(right_side)
    krylov_one = right_side / scale_norm
    margin_one = rhs_margin / scale_norm
    precond_one = precondition(krylov_one.astype(jnp.bfloat16), margin_one.astype(jnp.bfloat16))
    applied = apply_operator(precond_one)
    applied_margin = margin_of(applied)
    sums = allsum(
        jnp.stack(
            [
                jnp.sum(applied * krylov_one, axis=0),
                jnp.sum(applied * applied, axis=0),
                jnp.sum(krylov_one * krylov_one, axis=0),
            ]
        )
    )
    first_dot = sums[0]
    remainder = applied - first_dot * krylov_one
    expanded = sums[1] - 2.0 * first_dot * first_dot + first_dot * first_dot * sums[2]
    first_norm = guarded_norm(expanded, sums[1], remainder)
    krylov_two = remainder / first_norm
    margin_two = (applied_margin - first_dot * margin_one) / first_norm
    precond_two = precondition(krylov_two.astype(jnp.bfloat16), margin_two.astype(jnp.bfloat16))
    applied = apply_operator(precond_two)
    dots = allsum(
        jnp.stack(
            [
                jnp.sum(applied * krylov_one, axis=0),
                jnp.sum(applied * krylov_two, axis=0),
                jnp.sum(applied * applied, axis=0),
                jnp.sum(krylov_one * krylov_one, axis=0),
                jnp.sum(krylov_one * krylov_two, axis=0),
                jnp.sum(krylov_two * krylov_two, axis=0),
            ]
        )
    )
    cross_dot = dots[0]
    second_dot = dots[1]
    remainder = applied - cross_dot * krylov_one - second_dot * krylov_two
    expanded = (
        dots[2]
        - 2.0 * cross_dot * cross_dot
        - 2.0 * second_dot * second_dot
        + cross_dot * cross_dot * dots[3]
        + 2.0 * cross_dot * second_dot * dots[4]
        + second_dot * second_dot * dots[5]
    )
    second_norm = guarded_norm(expanded, dots[2], remainder)
    weight_one, weight_two, relative = least_squares(
        scale_norm, first_dot, first_norm, cross_dot, second_dot, second_norm
    )
    solution = weight_one * precond_one + weight_two * precond_two
    return (solution[None, None], relative)


def solution(mesh):
    return jax.shard_map(
        on_device,
        mesh=mesh,
        in_specs=(
            P("gx", "gy", None, None),
            P("gx", "gy", None, None),
            P("gx", "gy", None, None),
            P("gx", "gy", None, None, None),
            P("gx", "gy", None, None),
            P("gx", "gy", None, None),
            P("gx", "gy", None, None),
            P(),
        ),
        out_specs=(P("gx", "gy", None, None), P()),
        check_vma=False,
    )
```

```python
import jax
import numpy as np
import jax.numpy as jnp
from jax import lax
from jax.sharding import PartitionSpec as P

EPSILON = 1e-06
KEPT_SHARE = 1.0 / 64


def neighbours(rows, axis):
    count = lax.axis_size(axis)
    up = [(i, i + 1) for i in range(count - 1)]
    down = [(i + 1, i) for i in range(count - 1)]
    return lax.ppermute(rows[1], axis, up), lax.ppermute(rows[0], axis, down)


def exchange(packs):
    below_first, above_first = neighbours(packs[0:2], "gx")
    below_second, above_second = neighbours(packs[2:4], "gy")
    return jnp.stack([below_first, above_first, below_second, above_second], axis=0)


def allsum(value):
    value = lax.psum(value, "gy")
    for axis in ("gx",):
        count = lax.axis_size(axis)
        if count & (count - 1):
            value = lax.psum(value, axis)
            continue
        step = 1
        while step < count:
            value = value + lax.ppermute(value, axis, [(i, i ^ step) for i in range(count)])
            step *= 2
    return value


GATHER_ROUNDS = (
    ("gx", 32), ("gx", 16), ("gx", 8), ("gx", 4), ("gx", 2), ("gx", 1),
)


def gather_rounds(count_x, count_y):
    sizes = {"gx": count_x, "gy": count_y}
    return tuple((axis, step) for axis, step in GATHER_ROUNDS if step < sizes[axis])


def doubling_gather(block, rounds):
    held = block[None]
    for axis, step in rounds:
        count = lax.axis_size(axis)
        got = lax.ppermute(held, axis, [(i, i ^ step) for i in range(count)])
        upper = (lax.axis_index(axis) // step) % 2 == 1
        held = jnp.where(
            upper, jnp.concatenate([got, held], axis=0), jnp.concatenate([held, got], axis=0)
        )
    return lax.all_gather(held.reshape(-1, block.shape[-1]), "gy", axis=0, tiled=True)


def gathered_order(rounds, count_y):
    order = []
    for outer in range(count_y):
        for position in range(2 ** len(rounds)):
            index = {"gx": 0, "gy": outer}
            for bit, (axis, step) in enumerate(rounds):
                index[axis] += ((position >> bit) & 1) * step
            order.append(index["gx"] * count_y + index["gy"])
    return np.asarray(order, np.int32)


def least_squares(scale_norm, first_dot, first_norm, cross_dot, second_dot, second_norm):
    radius_one = jnp.sqrt(first_dot * first_dot + first_norm * first_norm)
    cosine_one = first_dot / radius_one
    sine_one = first_norm / radius_one
    upper_entry = cosine_one * cross_dot + sine_one * second_dot
    lower_entry = cosine_one * second_dot - sine_one * cross_dot
    radius_two = jnp.sqrt(lower_entry * lower_entry + second_norm * second_norm)
    cosine_two = lower_entry / radius_two
    sine_two = second_norm / radius_two
    weight_two = -cosine_two * sine_one * scale_norm / radius_two
    weight_one = (cosine_one * scale_norm - upper_entry * weight_two) / radius_one
    return (weight_one, weight_two, sine_one * sine_two)


def on_device(
    rhs,
    face_rows,
    margin_weight,
    local_blocks,
    subdomain_inverse,
    coarse_basis,
    coarse_inverse,
    coarse_map,
):
    right_side = rhs[0, 0]
    margin_rows = face_rows[0, 0]
    margin_weights = margin_weight[0, 0]
    local_block = local_blocks[0, 0]
    inverse_rows = subdomain_inverse[0, 0]
    basis = coarse_basis[0, 0]
    coarse_rows = coarse_inverse[0, 0]
    owned_rows = right_side.shape[0]
    system_count = right_side.shape[1]
    basis_count = basis.shape[1]
    block_rows = local_block.shape[1]
    count_x = lax.axis_size("gx")
    count_y = lax.axis_size("gy")
    rounds = gather_rounds(count_x, count_y)
    gathered_map = coarse_map[gathered_order(rounds, count_y)]
    selection = (
        gathered_map[:, None] == jnp.arange(gathered_map.shape[0], dtype=jnp.int32)[None, :]
    ).astype(jnp.bfloat16)

    def margin_of(field):
        return exchange(field[margin_rows])

    def coarse_gather(residual):
        return doubling_gather(residual, rounds)

    def precondition(rounded, margin):
        extended = jnp.concatenate([rounded, margin.reshape(-1, system_count)], axis=0)
        local_part = jnp.dot(inverse_rows, extended, preferred_element_type=jnp.float32)
        residual = lax.dot_general(
            basis, rounded, (((0,), (0,)), ((), ())), preferred_element_type=jnp.float32
        ).astype(jnp.bfloat16)
        gathered = coarse_gather(residual).reshape(selection.shape[0], -1)
        placed = lax.dot_general(
            selection, gathered, (((0,), (0,)), ((), ())), preferred_element_type=jnp.float32
        ).astype(jnp.bfloat16)
        solved = jnp.dot(
            coarse_rows, placed.reshape(-1, system_count), preferred_element_type=jnp.float32
        )
        return local_part + jnp.dot(
            basis, solved.astype(jnp.bfloat16), preferred_element_type=jnp.float32
        )

    def apply_operator(vector):
        rounded = vector.astype(jnp.bfloat16)
        own_part = jnp.einsum(
            "brc,bcn->brn",
            local_block,
            rounded.reshape(-1, block_rows, system_count),
            preferred_element_type=jnp.float32,
        ).reshape(owned_rows, system_count)
        weighted = margin_weights[:, :, None] * margin_of(rounded).astype(jnp.float32)
        coupling = (
            jnp.zeros((owned_rows, system_count), jnp.float32)
            .at[margin_rows.reshape(-1)]
            .add(weighted.reshape(-1, system_count))
        )
        return own_part - coupling

    def column_norm(vector):
        return jnp.sqrt(allsum(jnp.sum(vector * vector, axis=0)) + EPSILON)

    def guarded_norm(expanded, whole, remainder):
        kept = jnp.all(jnp.isfinite(expanded) & (expanded >= KEPT_SHARE * whole))
        return lax.cond(
            kept,
            lambda vector: jnp.sqrt(expanded + EPSILON),
            column_norm,
            remainder,
        )

    rhs_margin = margin_of(right_side)
    scale_norm = column_norm(right_side)
    krylov_one = right_side / scale_norm
    margin_one = rhs_margin / scale_norm
    precond_one = precondition(krylov_one.astype(jnp.bfloat16), margin_one.astype(jnp.bfloat16))
    applied = apply_operator(precond_one)
    applied_margin = margin_of(applied)
    sums = allsum(
        jnp.stack(
            [
                jnp.sum(applied * krylov_one, axis=0),
                jnp.sum(applied * applied, axis=0),
                jnp.sum(krylov_one * krylov_one, axis=0),
            ]
        )
    )
    first_dot = sums[0]
    remainder = applied - first_dot * krylov_one
    expanded = sums[1] - 2.0 * first_dot * first_dot + first_dot * first_dot * sums[2]
    first_norm = guarded_norm(expanded, sums[1], remainder)
    krylov_two = remainder / first_norm
    margin_two = (applied_margin - first_dot * margin_one) / first_norm
    precond_two = precondition(krylov_two.astype(jnp.bfloat16), margin_two.astype(jnp.bfloat16))
    applied = apply_operator(precond_two)
    dots = allsum(
        jnp.stack(
            [
                jnp.sum(applied * krylov_one, axis=0),
                jnp.sum(applied * krylov_two, axis=0),
                jnp.sum(applied * applied, axis=0),
                jnp.sum(krylov_one * krylov_one, axis=0),
                jnp.sum(krylov_one * krylov_two, axis=0),
                jnp.sum(krylov_two * krylov_two, axis=0),
            ]
        )
    )
    cross_dot = dots[0]
    second_dot = dots[1]
    remainder = applied - cross_dot * krylov_one - second_dot * krylov_two
    expanded = (
        dots[2]
        - 2.0 * cross_dot * cross_dot
        - 2.0 * second_dot * second_dot
        + cross_dot * cross_dot * dots[3]
        + 2.0 * cross_dot * second_dot * dots[4]
        + second_dot * second_dot * dots[5]
    )
    second_norm = guarded_norm(expanded, dots[2], remainder)
    weight_one, weight_two, relative = least_squares(
        scale_norm, first_dot, first_norm, cross_dot, second_dot, second_norm
    )
    solution = weight_one * precond_one + weight_two * precond_two
    return (solution[None, None], relative)


def solution(mesh):
    return jax.shard_map(
        on_device,
        mesh=mesh,
        in_specs=(
            P("gx", "gy", None, None),
            P("gx", "gy", None, None),
            P("gx", "gy", None, None),
            P("gx", "gy", None, None, None),
            P("gx", "gy", None, None),
            P("gx", "gy", None, None),
            P("gx", "gy", None, None),
            P(),
        ),
        out_specs=(P("gx", "gy", None, None), P()),
        check_vma=False,
    )
```
